256 devices in a mesh: doc: 16 (over z, core), term: 16 (over x, y).
Axes of the slice: x: 4, y: 4, z: 8, core: 2. Of those that a mesh axis runs over, the one named last changes fastest.
Arguments:
- tfidf: bfloat16 [8192, 32768], P('doc', 'term'), may hold values from 0.049804688 to 4
- occupancy: int32 [64, 256], P('doc', 'term'), may hold values 0 or 1
- doc_factor: bfloat16 [8192, 512], P(('doc', 'term')), as said below
- topic_factor: bfloat16 [32768, 512], P(('term', 'doc')), as said below
Outputs:
- new_docs: bfloat16 [8192, 512], P(('doc', 'term'))
- new_topics: bfloat16 [32768, 512], P(('term', 'doc'))
The draws below stay inside these ranges and needn't reach their ends.
Inputs may be any that keep to these rules, and one draw needn't show every extreme that they name: `doc_factor`: entries are positive, so gram_w is positive definite. `topic_factor`: entries are positive.
All inputs are finite; a program needn't handle non-finite values. No bound on the sum of `occupancy` on one device may be relied on, other than what follows from the above.
Results may differ from the reference program's by a relative error of at most 0.004.
Values may be sent and summed in bfloat16 or wider, within the bound.
No kernel may reach another device: no remote copies, remote signals or barrier semaphores. Data moves between devices by JAX's collectives and lax.ppermute only.
A program may use at most 64 MiB of HBM per device.

```python
import math
import jax
import jax.numpy as jnp
from jax import lax

RANK = 512
BLOCK = 64
TILE = 128
ROWS_DEV = 512
DOCS = 8192
TERMS = 32768
N_DOC = 16


def draw_doc_factor(key, part):
    base = jax.random.uniform(jax.random.fold_in(key, 11), (DOCS, RANK), jnp.float32, 0.1, 1.0)
    base = base * base * base * base
    position = jnp.arange(DOCS, dtype=jnp.float32)[:, None] / max(DOCS - 1, 1)
    scale = 1.0 + 2.0 * position
    return (base * scale * 2.0 / RANK).astype(jnp.bfloat16)


def draw_topic_factor(key, part):
    base = jax.random.uniform(jax.random.fold_in(key, 21), (TERMS, RANK), jnp.float32, 0.1, 1.0)
    base = base * base * base * base
    position = jnp.arange(TERMS, dtype=jnp.float32)[:, None] / max(TERMS - 1, 1)
    scale = (1.0 + 2.0 * position) / 2.0
    return (base * scale).astype(jnp.bfloat16)


def with_ends(array, key, least, largest):
    index_at = [jax.random.randint(jax.random.fold_in(key, axis), (), 0, length) for axis, length in enumerate(array.shape)]
    widest = array.shape.index(max(array.shape))
    beside = index_at[:widest] + [(index_at[widest] + 1) % array.shape[widest]] + index_at[widest + 1:]
    return array.at[tuple(index_at)].set(least).at[tuple(beside)].set(largest)


def level_of(key, dims, shards, low, top_value):
    def one(dim, parts):
        steps = jax.random.uniform(jax.random.fold_in(jax.random.fold_in(key, 6), dim), (parts,), jnp.float32, low / len(shards), top_value / len(shards))
        return jnp.repeat(jnp.exp(steps), dims[dim] // parts).reshape((-1,) + (1,) * (len(dims) - dim - 1))

    loudness = one(*shards[0])
    for cut in shards[1:]:
        loudness = loudness * one(*cut)
    return loudness


def setup_inputs(seed: int = 0) -> dict:
    seeds = jax.random.split(jax.random.key(seed), 5)
    return {
        "tfidf": jnp.clip(jnp.exp(math.log(4.0) - 4.3859405 * jax.random.uniform(seeds[0], (DOCS, TERMS), jnp.float32) ** level_of(seeds[0], (DOCS, TERMS), ((0, 16), (1, 16)), -0.2, 0.2)), 0.049804688, 4.0).astype(jnp.bfloat16),
        "occupancy": with_ends((jax.random.randint(seeds[1], (DOCS // TILE, TERMS // TILE), 0, 4) < 3).astype(jnp.int32), jax.random.fold_in(seeds[1], 1), 0, 1),
        "doc_factor": draw_doc_factor(jax.random.fold_in(seeds[4], 71), 0),
        "topic_factor": draw_topic_factor(jax.random.fold_in(seeds[4], 71), 0),
    }


def mask_tiles(block, occ):
    rows, cols = block.shape
    tiles = block.reshape(rows // TILE, TILE, cols // TILE, TILE)
    tiles = tiles * occ.astype(jnp.bfloat16)[:, None, :, None]
    return tiles.reshape(rows, cols)

def block_sweep(factor, cross, gram):
    eye = jnp.eye(BLOCK, dtype=jnp.float32)

    def one_block(index, current):
        lo = (index * BLOCK).astype(jnp.int32)
        part = lax.dynamic_slice(gram, (lo, lo), (BLOCK, BLOCK))
        lower = jnp.linalg.cholesky(part)
        inverse = jax.scipy.linalg.cho_solve((lower, True), eye)
        columns = lax.dynamic_slice_in_dim(gram, lo, BLOCK, 1)
        target = lax.dynamic_slice_in_dim(cross, lo, BLOCK, 1)
        old_cols = lax.dynamic_slice_in_dim(current, lo, BLOCK, 1)
        resid = target - jnp.dot(current, columns, precision=lax.Precision.HIGHEST)
        fresh = old_cols + jnp.dot(resid, inverse, precision=lax.Precision.HIGHEST)
        return lax.dynamic_update_slice_in_dim(current, jnp.maximum(fresh, 0.0), lo, 1)
    return lax.fori_loop(jnp.int32(0), jnp.int32(RANK // BLOCK), one_block, factor)

def reference(tfidf, occupancy, doc_factor, topic_factor):
    groups_x = tfidf.reshape(N_DOC, ROWS_DEV, TERMS)
    groups_m = occupancy.reshape(N_DOC, ROWS_DEV // TILE, TERMS // TILE)
    groups_w = doc_factor.reshape(N_DOC, ROWS_DEV, RANK)

    def add_group(total, item):
        block, occ, rows_w = item
        masked = mask_tiles(block, occ)
        part = lax.dot_general(masked.astype(jnp.float32), rows_w.astype(jnp.float32), (((0,), (0,)), ((), ())), preferred_element_type=jnp.float32)
        return (total + part, None)
    cross_h, unused = lax.scan(add_group, jnp.zeros((TERMS, RANK), jnp.float32), (groups_x, groups_m, groups_w))
    gram_w = jnp.dot(doc_factor.T.astype(jnp.float32), doc_factor.astype(jnp.float32), preferred_element_type=jnp.float32)
    topic_work = block_sweep(topic_factor.astype(jnp.float32), cross_h, gram_w)
    new_topics = topic_work.astype(jnp.bfloat16)

    def doc_group(carry, item):
        block, occ = item
        masked = mask_tiles(block, occ)
        return (carry, jnp.dot(masked.astype(jnp.float32), new_topics.astype(jnp.float32), preferred_element_type=jnp.float32))
    unused2, cross_w = lax.scan(doc_group, jnp.zeros((), jnp.float32), (groups_x, groups_m))
    cross_w = cross_w.reshape(DOCS, RANK)
    gram_h = jnp.dot(new_topics.T.astype(jnp.float32), new_topics.astype(jnp.float32), preferred_element_type=jnp.float32)
    doc_work = block_sweep(doc_factor.astype(jnp.float32), cross_w, gram_h)
    return (doc_work.astype(jnp.bfloat16), new_topics)
```

```python
import jax
import jax.numpy as jnp
from jax import lax
from jax.sharding import PartitionSpec as P

BLOCK = 64
TILE = 128


def mask_tiles(block, occ):
    rows, cols = block.shape
    tiles = block.reshape(rows // TILE, TILE, cols // TILE, TILE)
    tiles = tiles * occ.astype(jnp.bfloat16)[:, None, :, None]
    return tiles.reshape(rows, cols)


def block_inverses(gram):
    n = gram.shape[0] // BLOCK
    diag = jnp.stack([gram[b * BLOCK:(b + 1) * BLOCK, b * BLOCK:(b + 1) * BLOCK] for b in range(n)])
    lower = jnp.linalg.cholesky(diag)
    eye = jnp.broadcast_to(jnp.eye(BLOCK, dtype=jnp.float32), diag.shape)
    return jax.scipy.linalg.cho_solve((lower, True), eye)


def block_sweep(factor, cross, gram, inverses):
    n = gram.shape[0] // BLOCK
    current = factor
    for b in range(n):
        lo, hi = b * BLOCK, (b + 1) * BLOCK
        resid = cross[:, lo:hi] - jnp.dot(current, gram[:, lo:hi], precision=lax.Precision.HIGHEST)
        fresh = current[:, lo:hi] + jnp.dot(resid, inverses[b], precision=lax.Precision.HIGHEST)
        current = lax.dynamic_update_slice_in_dim(current, jnp.maximum(fresh, 0.0), lo, 1)
    return current


def shards(tfidf, occupancy, doc_factor, topic_factor):
    masked = mask_tiles(tfidf, occupancy)
    rows_group = lax.all_gather(doc_factor, "term", axis=0, tiled=True)
    gram_w = lax.psum(
        lax.dot_general(rows_group, rows_group, (((0,), (0,)), ((), ())), preferred_element_type=jnp.float32),
        "doc",
    )
    inv_w = block_inverses(gram_w)
    cross_h = lax.psum_scatter(
        lax.dot_general(
            masked, rows_group, (((0,), (0,)), ((), ())), preferred_element_type=jnp.float32
        ),
        "doc",
        scatter_dimension=0,
        tiled=True,
    )
    new_topics = block_sweep(topic_factor.astype(jnp.float32), cross_h, gram_w, inv_w).astype(jnp.bfloat16)
    topic_group = lax.all_gather(new_topics, "doc", axis=0, tiled=True)
    gram_h = lax.psum(
        lax.dot_general(topic_group, topic_group, (((0,), (0,)), ((), ())), preferred_element_type=jnp.float32),
        "term",
    )
    inv_h = block_inverses(gram_h)
    cross_w = lax.psum_scatter(
        jnp.dot(masked, topic_group, preferred_element_type=jnp.float32),
        "term",
        scatter_dimension=0,
        tiled=True,
    )
    new_docs = block_sweep(doc_factor.astype(jnp.float32), cross_w, gram_h, inv_h).astype(jnp.bfloat16)
    return (new_docs, new_topics)


def solution(mesh):
    placed = (
        P("doc", "term"),
        P("doc", "term"),
        P(("doc", "term"), None),
        P(("term", "doc"), None),
    )
    return jax.shard_map(
        shards,
        mesh=mesh,
        in_specs=placed,
        out_specs=(P(("doc", "term"), None), P(("term", "doc"), None)),
        check_vma=False,
    )
```

```python
import jax
import jax.numpy as jnp
from jax import lax
from jax.experimental import pallas as pl
from jax.sharding import PartitionSpec as P

BLOCK = 64
TILE = 128


def mask_tiles(block, occ):
    rows, cols = block.shape
    tiles = block.reshape(rows // TILE, TILE, cols // TILE, TILE)
    tiles = tiles * occ.astype(jnp.bfloat16)[:, None, :, None]
    return tiles.reshape(rows, cols)


def _elim_kernel(m_ref, o_ref):
    n = m_ref.shape[0]
    rows = [m_ref[i] for i in range(n)]
    for j in range(n):
        root = jnp.sqrt(rows[j][:, j:j + 1])
        pivot = rows[j] / root
        rows[j] = pivot
        for i in range(j + 1, n):
            rows[i] = rows[i] - (rows[i][:, j:j + 1] / root) * pivot
    for i in range(n):
        o_ref[i] = rows[i][:, n:]


def block_inverses(gram):
    n = gram.shape[0] // BLOCK
    diag = jnp.stack([gram[b * BLOCK:(b + 1) * BLOCK, b * BLOCK:(b + 1) * BLOCK] for b in range(n)])
    eye = jnp.broadcast_to(jnp.eye(BLOCK, dtype=jnp.float32), diag.shape)
    aug = jnp.transpose(jnp.concatenate([diag, eye], axis=-1), (1, 0, 2))
    inv_lower = pl.pallas_call(
        _elim_kernel,
        out_shape=jax.ShapeDtypeStruct((BLOCK, n, BLOCK), jnp.float32),
    )(aug)
    return jnp.einsum("kbi,kbj->bij", inv_lower, inv_lower, precision=lax.Precision.HIGHEST)


def butterfly_psum(x, axis, order):
    size = lax.axis_size(axis)
    idx = lax.axis_index(axis)
    cur = x
    for k in order:
        half = cur.shape[0] // 2
        upper = ((idx >> k) & 1) == 1
        lo, hi = cur[:half], cur[half:]
        send = jnp.where(upper, lo, hi)
        keep = jnp.where(upper, hi, lo)
        got = lax.ppermute(send, axis, [(i, i ^ (1 << k)) for i in range(size)])
        cur = keep + got
    for k in reversed(order):
        upper = ((idx >> k) & 1) == 1
        got = lax.ppermute(cur, axis, [(i, i ^ (1 << k)) for i in range(size)])
        cur = jnp.where(upper, jnp.concatenate([got, cur]), jnp.concatenate([cur, got]))
    return cur


def block_sweep(factor, cross, gram, inverses):
    n = gram.shape[0] // BLOCK
    current = factor
    for b in range(n):
        lo, hi = b * BLOCK, (b + 1) * BLOCK
        resid = cross[:, lo:hi] - jnp.dot(current, gram[:, lo:hi], precision=lax.Precision.HIGHEST)
        fresh = current[:, lo:hi] + jnp.dot(resid, inverses[b], precision=lax.Precision.HIGHEST)
        current = lax.dynamic_update_slice_in_dim(current, jnp.maximum(fresh, 0.0), lo, 1)
    return current


def shards(tfidf, occupancy, doc_factor, topic_factor):
    masked = mask_tiles(tfidf, occupancy)
    rows_group = lax.all_gather(doc_factor, "term", axis=0, tiled=True)
    gram_w = butterfly_psum(
        lax.dot_general(rows_group, rows_group, (((0,), (0,)), ((), ())), preferred_element_type=jnp.float32),
        "doc",
        (0, 1, 2, 3),
    )
    inv_w = block_inverses(gram_w)
    cross_h = lax.psum_scatter(
        lax.dot_general(
            masked, rows_group, (((0,), (0,)), ((), ())), preferred_element_type=jnp.float32
        ),
        "doc",
        scatter_dimension=0,
        tiled=True,
    )
    new_topics = block_sweep(topic_factor.astype(jnp.float32), cross_h, gram_w, inv_w).astype(jnp.bfloat16)
    topic_group = lax.all_gather(new_topics, "doc", axis=0, tiled=True)
    gram_h = butterfly_psum(
        lax.dot_general(topic_group, topic_group, (((0,), (0,)), ((), ())), preferred_element_type=jnp.float32),
        "term",
        (0, 2, 1, 3),
    )
    inv_h = block_inverses(gram_h)
    cross_w = lax.psum_scatter(
        jnp.dot(masked, topic_group, preferred_element_type=jnp.float32),
        "term",
        scatter_dimension=0,
        tiled=True,
    )
    new_docs = block_sweep(doc_factor.astype(jnp.float32), cross_w, gram_h, inv_h).astype(jnp.bfloat16)
    return (new_docs, new_topics)


def solution(mesh):
    placed = (
        P("doc", "term"),
        P("doc", "term"),
        P(("doc", "term"), None),
        P(("term", "doc"), None),
    )
    return jax.shard_map(
        shards,
        mesh=mesh,
        in_specs=placed,
        out_specs=(P(("doc", "term"), None), P(("term", "doc"), None)),
        check_vma=False,
    )
```

```python
import jax
import jax.numpy as jnp
from jax import lax
from jax.experimental import pallas as pl
from jax.sharding import PartitionSpec as P

BLOCK = 64
TILE = 128


def mask_tiles(block, occ):
    rows, cols = block.shape
    tiles = block.reshape(rows // TILE, TILE, cols // TILE, TILE)
    tiles = tiles * occ.astype(jnp.bfloat16)[:, None, :, None]
    return tiles.reshape(rows, cols)


def _elim_kernel(m_ref, o_ref):
    n = m_ref.shape[0]
    rows = [m_ref[i] for i in range(n)]
    for j in range(n):
        root = jnp.sqrt(rows[j][:, j:j + 1])
        pivot = rows[j] / root
        rows[j] = pivot
        for i in range(j + 1, n):
            rows[i] = rows[i] - (rows[i][:, j:j + 1] / root) * pivot
    for i in range(n):
        o_ref[i] = rows[i][:, n:]


def block_inverses(gram):
    n = gram.shape[0] // BLOCK
    diag = jnp.stack([gram[b * BLOCK:(b + 1) * BLOCK, b * BLOCK:(b + 1) * BLOCK] for b in range(n)])
    eye = jnp.broadcast_to(jnp.eye(BLOCK, dtype=jnp.float32), diag.shape)
    aug = jnp.transpose(jnp.concatenate([diag, eye], axis=-1), (1, 0, 2))
    inv_lower = pl.pallas_call(
        _elim_kernel,
        out_shape=jax.ShapeDtypeStruct((BLOCK, n, BLOCK), jnp.float32),
    )(aug)
    return jnp.einsum("kbi,kbj->bij", inv_lower, inv_lower, precision=lax.Precision.HIGHEST)


def butterfly_psum(x, axis, order):
    size = lax.axis_size(axis)
    idx = lax.axis_index(axis)
    cur = x
    for k in order:
        half = cur.shape[0] // 2
        upper = ((idx >> k) & 1) == 1
        lo, hi = cur[:half], cur[half:]
        send = jnp.where(upper, lo, hi)
        keep = jnp.where(upper, hi, lo)
        got = lax.ppermute(send, axis, [(i, i ^ (1 << k)) for i in range(size)])
        cur = keep + got
    for k in reversed(order):
        upper = ((idx >> k) & 1) == 1
        got = lax.ppermute(cur, axis, [(i, i ^ (1 << k)) for i in range(size)])
        cur = jnp.where(upper, jnp.concatenate([got, cur]), jnp.concatenate([cur, got]))
    return cur


def block_sweep(factor, cross, gram, inverses):
    n = gram.shape[0] // BLOCK
    current = factor
    for b in range(n):
        lo, hi = b * BLOCK, (b + 1) * BLOCK
        resid = cross[:, lo:hi] - jnp.dot(current, gram[:, lo:hi], precision=lax.Precision.HIGHEST)
        fresh = current[:, lo:hi] + jnp.dot(resid, inverses[b], precision=lax.Precision.HIGHEST)
        current = lax.dynamic_update_slice_in_dim(current, jnp.maximum(fresh, 0.0), lo, 1)
    return current


def shards(tfidf, occupancy, doc_factor, topic_factor):
    masked = mask_tiles(tfidf, occupancy)
    rows_group = lax.all_gather(doc_factor, "term", axis=0, tiled=True)
    gram_w = butterfly_psum(
        lax.dot_general(rows_group, rows_group, (((0,), (0,)), ((), ())), preferred_element_type=jnp.float32),
        "doc",
        (0, 1, 2, 3),
    )
    inv_w = block_inverses(gram_w)
    cross_h = lax.psum_scatter(
        lax.dot_general(
            masked, rows_group, (((0,), (0,)), ((), ())), preferred_element_type=jnp.float32
        ),
        "doc",
        scatter_dimension=0,
        tiled=True,
    )
    new_topics = block_sweep(topic_factor.astype(jnp.float32), cross_h, gram_w, inv_w).astype(jnp.bfloat16)
    topic_group = lax.all_gather(new_topics, "doc", axis=0, tiled=True)
    cross_part = jnp.dot(masked, topic_group, preferred_element_type=jnp.float32)
    cross_part, topic_group = lax.optimization_barrier((cross_part, topic_group))
    gram_h = butterfly_psum(
        lax.dot_general(topic_group, topic_group, (((0,), (0,)), ((), ())), preferred_element_type=jnp.float32),
        "term",
        (0, 2, 1, 3),
    )
    inv_h = block_inverses(gram_h)
    cross_w = lax.psum_scatter(
        cross_part,
        "term",
        scatter_dimension=0,
        tiled=True,
    )
    new_docs = block_sweep(doc_factor.astype(jnp.float32), cross_w, gram_h, inv_h).astype(jnp.bfloat16)
    return (new_docs, new_topics)


def solution(mesh):
    placed = (
        P("doc", "term"),
        P("doc", "term"),
        P(("doc", "term"), None),
        P(("term", "doc"), None),
    )
    return jax.shard_map(
        shards,
        mesh=mesh,
        in_specs=placed,
        out_specs=(P(("doc", "term"), None), P(("term", "doc"), None)),
        check_vma=False,
    )
```

```python
import jax
import jax.numpy as jnp
from jax import lax
from jax.experimental import pallas as pl
from jax.sharding import PartitionSpec as P

BLOCK = 64
TILE = 128


def mask_tiles(block, occ):
    rows, cols = block.shape
    tiles = block.reshape(rows // TILE, TILE, cols // TILE, TILE)
    tiles = tiles * occ.astype(jnp.bfloat16)[:, None, :, None]
    return tiles.reshape(rows, cols)


def _elim_kernel(m_ref, o_ref):
    n = m_ref.shape[0]
    rows = [m_ref[i] for i in range(n)]
    for j in range(n):
        root = jnp.sqrt(rows[j][:, j:j + 1])
        pivot = rows[j] / root
        rows[j] = pivot
        for i in range(j + 1, n):
            rows[i] = rows[i] - (rows[i][:, j:j + 1] / root) * pivot
    for i in range(n):
        o_ref[i] = rows[i][:, n:]


def block_inverses(gram):
    n = gram.shape[0] // BLOCK
    diag = jnp.stack([gram[b * BLOCK:(b + 1) * BLOCK, b * BLOCK:(b + 1) * BLOCK] for b in range(n)])
    eye = jnp.broadcast_to(jnp.eye(BLOCK, dtype=jnp.float32), diag.shape)
    aug = jnp.transpose(jnp.concatenate([diag, eye], axis=-1), (1, 0, 2))
    inv_lower = pl.pallas_call(
        _elim_kernel,
        out_shape=jax.ShapeDtypeStruct((BLOCK, n, BLOCK), jnp.float32),
    )(aug)
    return jnp.einsum("kbi,kbj->bij", inv_lower, inv_lower, precision=lax.Precision.HIGHEST)


def _partners(size, shift, m):
    return [(i, i ^ (m << shift)) for i in range(size)]


def radix4_scatter(x, axis, shifts):
    size = lax.axis_size(axis)
    idx = lax.axis_index(axis)
    cur = x
    for s in shifts:
        q = cur.shape[0] // 4
        digit = (idx >> s) & 3
        acc = lax.dynamic_slice_in_dim(cur, digit * q, q)
        for m in (1, 2, 3):
            send = lax.dynamic_slice_in_dim(cur, (digit ^ m) * q, q)
            acc = acc + lax.ppermute(send, axis, _partners(size, s, m))
        cur = acc
    return cur


def radix4_gather(x, axis, shifts):
    size = lax.axis_size(axis)
    idx = lax.axis_index(axis)
    cur = x
    for s in reversed(shifts):
        digit = (idx >> s) & 3
        got = [cur] + [lax.ppermute(cur, axis, _partners(size, s, m)) for m in (1, 2, 3)]
        pieces = []
        for p in range(4):
            rel = digit ^ p
            pieces.append(jnp.where(rel == 0, got[0], jnp.where(rel == 1, got[1], jnp.where(rel == 2, got[2], got[3]))))
        cur = jnp.concatenate(pieces)
    return cur


def block_sweep(factor, cross, gram, inverses):
    n = gram.shape[0] // BLOCK
    current = factor
    for b in range(n):
        lo, hi = b * BLOCK, (b + 1) * BLOCK
        resid = cross[:, lo:hi] - jnp.dot(current, gram[:, lo:hi], precision=lax.Precision.HIGHEST)
        fresh = current[:, lo:hi] + jnp.dot(resid, inverses[b], precision=lax.Precision.HIGHEST)
        current = lax.dynamic_update_slice_in_dim(current, jnp.maximum(fresh, 0.0), lo, 1)
    return current


def shards(tfidf, occupancy, doc_factor, topic_factor):
    masked = mask_tiles(tfidf, occupancy)
    rows_group = lax.all_gather(doc_factor, "term", axis=0, tiled=True)
    gram_w = radix4_gather(
        radix4_scatter(
            lax.dot_general(rows_group, rows_group, (((0,), (0,)), ((), ())), preferred_element_type=jnp.float32),
            "doc",
            (0, 2),
        ),
        "doc",
        (0, 2),
    )
    inv_w = block_inverses(gram_w)
    cross_h = lax.psum_scatter(
        lax.dot_general(
            masked, rows_group, (((0,), (0,)), ((), ())), preferred_element_type=jnp.float32
        ),
        "doc",
        scatter_dimension=0,
        tiled=True,
    )
    new_topics = block_sweep(topic_factor.astype(jnp.float32), cross_h, gram_w, inv_w).astype(jnp.bfloat16)
    topic_group = lax.all_gather(new_topics, "doc", axis=0, tiled=True)
    cross_part = jnp.dot(masked, topic_group, preferred_element_type=jnp.float32)
    gram_part = lax.dot_general(topic_group, topic_group, (((0,), (0,)), ((), ())), preferred_element_type=jnp.float32)
    n_term = lax.axis_size("term")
    packed = jnp.stack(
        [cross_part.reshape(n_term, -1, cross_part.shape[1]), gram_part.reshape(n_term, -1, gram_part.shape[1])], axis=1
    ).reshape(-1, gram_part.shape[1])
    chunk = radix4_scatter(packed, "term", (2, 0))
    cross_w = chunk[: chunk.shape[0] // 2]
    gram_h = radix4_gather(chunk[chunk.shape[0] // 2:], "term", (2, 0))
    inv_h = block_inverses(gram_h)
    new_docs = block_sweep(doc_factor.astype(jnp.float32), cross_w, gram_h, inv_h).astype(jnp.bfloat16)
    return (new_docs, new_topics)


def solution(mesh):
    placed = (
        P("doc", "term"),
        P("doc", "term"),
        P(("doc", "term"), None),
        P(("term", "doc"), None),
    )
    return jax.shard_map(
        shards,
        mesh=mesh,
        in_specs=placed,
        out_specs=(P(("doc", "term"), None), P(("term", "doc"), None)),
        check_vma=False,
    )
```

```python
import jax
import jax.numpy as jnp
from jax import lax
from jax.experimental import pallas as pl
from jax.sharding import PartitionSpec as P

BLOCK = 64
TILE = 128


def mask_tiles(block, occ):
    rows, cols = block.shape
    tiles = block.reshape(rows // TILE, TILE, cols // TILE, TILE)
    tiles = tiles * occ.astype(jnp.bfloat16)[:, None, :, None]
    return tiles.reshape(rows, cols)


def _elim_kernel(m_ref, o_ref):
    n = m_ref.shape[0]
    rows = [m_ref[i] for i in range(n)]
    for j in range(n):
        root = jnp.sqrt(rows[j][:, j:j + 1])
        pivot = rows[j] / root
        rows[j] = pivot
        scaled = pivot / root
        for i in range(j + 1, n):
            rows[i] = rows[i] - rows[i][:, j:j + 1] * scaled
    for i in range(n):
        o_ref[i] = rows[i][:, n:]


def block_inverses(gram):
    n = gram.shape[0] // BLOCK
    diag = jnp.stack([gram[b * BLOCK:(b + 1) * BLOCK, b * BLOCK:(b + 1) * BLOCK] for b in range(n)])
    eye = jnp.broadcast_to(jnp.eye(BLOCK, dtype=jnp.float32), diag.shape)
    aug = jnp.transpose(jnp.concatenate([diag, eye], axis=-1), (1, 0, 2))
    inv_lower = pl.pallas_call(
        _elim_kernel,
        out_shape=jax.ShapeDtypeStruct((BLOCK, n, BLOCK), jnp.float32),
    )(aug)
    return jnp.einsum("kbi,kbj->bij", inv_lower, inv_lower, precision=lax.Precision.HIGHEST)


def _partners(size, shift, m):
    return [(i, i ^ (m << shift)) for i in range(size)]


def radix4_scatter(x, axis, shifts):
    size = lax.axis_size(axis)
    idx = lax.axis_index(axis)
    cur = x
    for s in shifts:
        q = cur.shape[0] // 4
        digit = (idx >> s) & 3
        acc = lax.dynamic_slice_in_dim(cur, digit * q, q)
        for m in (1, 2, 3):
            send = lax.dynamic_slice_in_dim(cur, (digit ^ m) * q, q)
            acc = acc + lax.ppermute(send, axis, _partners(size, s, m))
        cur = acc
    return cur


def radix4_gather(x, axis, shifts):
    size = lax.axis_size(axis)
    idx = lax.axis_index(axis)
    cur = x
    for s in reversed(shifts):
        digit = (idx >> s) & 3
        got = [cur] + [lax.ppermute(cur, axis, _partners(size, s, m)) for m in (1, 2, 3)]
        pieces = []
        for p in range(4):
            rel = digit ^ p
            pieces.append(jnp.where(rel == 0, got[0], jnp.where(rel == 1, got[1], jnp.where(rel == 2, got[2], got[3]))))
        cur = jnp.concatenate(pieces)
    return cur


def block_sweep(factor, cross, gram, inverses):
    n = gram.shape[0] // BLOCK
    current = factor
    for b in range(n):
        lo, hi = b * BLOCK, (b + 1) * BLOCK
        resid = cross[:, lo:hi] - jnp.dot(current, gram[:, lo:hi], precision=lax.Precision.HIGHEST)
        fresh = current[:, lo:hi] + jnp.dot(resid, inverses[b], precision=lax.Precision.HIGHEST)
        current = lax.dynamic_update_slice_in_dim(current, jnp.maximum(fresh, 0.0), lo, 1)
    return current


def shards(tfidf, occupancy, doc_factor, topic_factor):
    masked = mask_tiles(tfidf, occupancy)
    rows_group = lax.all_gather(doc_factor, "term", axis=0, tiled=True)
    gram_w = radix4_gather(
        radix4_scatter(
            lax.dot_general(rows_group, rows_group, (((0,), (0,)), ((), ())), preferred_element_type=jnp.float32),
            "doc",
            (0, 2),
        ),
        "doc",
        (0, 2),
    )
    inv_w = block_inverses(gram_w)
    cross_h = lax.psum_scatter(
        lax.dot_general(
            masked, rows_group, (((0,), (0,)), ((), ())), preferred_element_type=jnp.float32
        ),
        "doc",
        scatter_dimension=0,
        tiled=True,
    )
    new_topics = block_sweep(topic_factor.astype(jnp.float32), cross_h, gram_w, inv_w).astype(jnp.bfloat16)
    topic_group = lax.all_gather(new_topics, "doc", axis=0, tiled=True)
    cross_part = jnp.dot(masked, topic_group, preferred_element_type=jnp.float32)
    gram_part = lax.dot_general(topic_group, topic_group, (((0,), (0,)), ((), ())), preferred_element_type=jnp.float32)
    n_term = lax.axis_size("term")
    packed = jnp.stack(
        [cross_part.reshape(n_term, -1, cross_part.shape[1]), gram_part.reshape(n_term, -1, gram_part.shape[1])], axis=1
    ).reshape(-1, gram_part.shape[1])
    chunk = radix4_scatter(packed, "term", (2, 0))
    cross_w = chunk[: chunk.shape[0] // 2]
    gram_h = radix4_gather(chunk[chunk.shape[0] // 2:], "term", (2, 0))
    inv_h = block_inverses(gram_h)
    new_docs = block_sweep(doc_factor.astype(jnp.float32), cross_w, gram_h, inv_h).astype(jnp.bfloat16)
    return (new_docs, new_topics)


def solution(mesh):
    placed = (
        P("doc", "term"),
        P("doc", "term"),
        P(("doc", "term"), None),
        P(("term", "doc"), None),
    )
    return jax.shard_map(
        shards,
        mesh=mesh,
        in_specs=placed,
        out_specs=(P(("doc", "term"), None), P(("term", "doc"), None)),
        check_vma=False,
    )
```

```python
import jax
import jax.numpy as jnp
from jax import lax
from jax.experimental import pallas as pl
from jax.sharding import PartitionSpec as P

BLOCK = 64
TILE = 128


def mask_tiles(block, occ):
    rows, cols = block.shape
    tiles = block.reshape(rows // TILE, TILE, cols // TILE, TILE)
    tiles = tiles * occ.astype(jnp.bfloat16)[:, None, :, None]
    return tiles.reshape(rows, cols)


def _elim_kernel(m_ref, o_ref):
    n = m_ref.shape[0]
    rows = [m_ref[i] for i in range(n)]
    for j in range(n):
        root = jnp.sqrt(rows[j][:, j:j + 1])
        pivot = rows[j] / root
        rows[j] = pivot
        scaled = pivot / root
        for i in range(j + 1, n):
            rows[i] = rows[i] - rows[i][:, j:j + 1] * scaled
    for i in range(n):
        o_ref[i] = rows[i][:, n:]


def block_inverses(gram):
    n = gram.shape[0] // BLOCK
    diag = jnp.stack([gram[b * BLOCK:(b + 1) * BLOCK, b * BLOCK:(b + 1) * BLOCK] for b in range(n)])
    eye = jnp.broadcast_to(jnp.eye(BLOCK, dtype=jnp.float32), diag.shape)
    aug = jnp.transpose(jnp.concatenate([diag, eye], axis=-1), (1, 0, 2))
    inv_lower = pl.pallas_call(
        _elim_kernel,
        out_shape=jax.ShapeDtypeStruct((BLOCK, n, BLOCK), jnp.float32),
    )(aug)
    return jnp.einsum("kbi,kbj->bji", inv_lower, inv_lower, precision=lax.Precision.HIGHEST)


def _partners(size, shift, m):
    return [(i, i ^ (m << shift)) for i in range(size)]


def radix4_scatter(x, axis, shifts):
    size = lax.axis_size(axis)
    idx = lax.axis_index(axis)
    cur = x
    for s in shifts:
        q = cur.shape[0] // 4
        digit = (idx >> s) & 3
        acc = lax.dynamic_slice_in_dim(cur, digit * q, q)
        for m in (1, 2, 3):
            send = lax.dynamic_slice_in_dim(cur, (digit ^ m) * q, q)
            acc = acc + lax.ppermute(send, axis, _partners(size, s, m))
        cur = acc
    return cur


def radix4_gather(x, axis, shifts):
    size = lax.axis_size(axis)
    idx = lax.axis_index(axis)
    cur = x
    for s in reversed(shifts):
        digit = (idx >> s) & 3
        got = [cur] + [lax.ppermute(cur, axis, _partners(size, s, m)) for m in (1, 2, 3)]
        pieces = []
        for p in range(4):
            rel = digit ^ p
            pieces.append(jnp.where(rel == 0, got[0], jnp.where(rel == 1, got[1], jnp.where(rel == 2, got[2], got[3]))))
        cur = jnp.concatenate(pieces)
    return cur


def _sweep_kernel(ft_ref, ct_ref, g_ref, it_ref, o_ref):
    n = g_ref.shape[0] // BLOCK
    o_ref[...] = ft_ref[...]
    for b in range(n):
        lo, hi = b * BLOCK, (b + 1) * BLOCK
        prod = jnp.dot(g_ref[lo:hi, :], o_ref[...], precision=lax.Precision.HIGHEST, preferred_element_type=jnp.float32)
        resid = ct_ref[lo:hi, :] - prod
        step = jnp.dot(it_ref[b], resid, precision=lax.Precision.HIGHEST, preferred_element_type=jnp.float32)
        o_ref[lo:hi, :] = jnp.maximum(o_ref[lo:hi, :] + step, 0.0)


def block_sweep(factor, cross, gram, inverses_t):
    out_t = pl.pallas_call(
        _sweep_kernel,
        out_shape=jax.ShapeDtypeStruct((factor.shape[1], factor.shape[0]), jnp.float32),
    )(factor.T, cross.T, gram, inverses_t)
    return out_t.T


def shards(tfidf, occupancy, doc_factor, topic_factor):
    masked = mask_tiles(tfidf, occupancy)
    rows_group = lax.all_gather(doc_factor, "term", axis=0, tiled=True)
    gram_w = radix4_gather(
        radix4_scatter(
            lax.dot_general(rows_group, rows_group, (((0,), (0,)), ((), ())), preferred_element_type=jnp.float32),
            "doc",
            (0, 2),
        ),
        "doc",
        (0, 2),
    )
    inv_w = block_inverses(gram_w)
    cross_h = lax.psum_scatter(
        lax.dot_general(
            masked, rows_group, (((0,), (0,)), ((), ())), preferred_element_type=jnp.float32
        ),
        "doc",
        scatter_dimension=0,
        tiled=True,
    )
    new_topics = block_sweep(topic_factor.astype(jnp.float32), cross_h, gram_w, inv_w).astype(jnp.bfloat16)
    topic_group = lax.all_gather(new_topics, "doc", axis=0, tiled=True)
    cross_part = jnp.dot(masked, topic_group, preferred_element_type=jnp.float32)
    gram_part = lax.dot_general(topic_group, topic_group, (((0,), (0,)), ((), ())), preferred_element_type=jnp.float32)
    n_term = lax.axis_size("term")
    packed = jnp.stack(
        [cross_part.reshape(n_term, -1, cross_part.shape[1]), gram_part.reshape(n_term, -1, gram_part.shape[1])], axis=1
    ).reshape(-1, gram_part.shape[1])
    chunk = radix4_scatter(packed, "term", (2, 0))
    cross_w = chunk[: chunk.shape[0] // 2]
    gram_h = radix4_gather(chunk[chunk.shape[0] // 2:], "term", (2, 0))
    inv_h = block_inverses(gram_h)
    new_docs = block_sweep(doc_factor.astype(jnp.float32), cross_w, gram_h, inv_h).astype(jnp.bfloat16)
    return (new_docs, new_topics)


def solution(mesh):
    placed = (
        P("doc", "term"),
        P("doc", "term"),
        P(("doc", "term"), None),
        P(("term", "doc"), None),
    )
    return jax.shard_map(
        shards,
        mesh=mesh,
        in_specs=placed,
        out_specs=(P(("doc", "term"), None), P(("term", "doc"), None)),
        check_vma=False,
    )
```

```python
import jax
import jax.numpy as jnp
from jax import lax
from jax.experimental import pallas as pl
from jax.sharding import PartitionSpec as P

BLOCK = 64
TILE = 128


def mask_tiles(block, occ):
    rows, cols = block.shape
    tiles = block.reshape(rows // TILE, TILE, cols // TILE, TILE)
    tiles = tiles * occ.astype(jnp.bfloat16)[:, None, :, None]
    return tiles.reshape(rows, cols)


def _elim_kernel(m_ref, o_ref):
    n = m_ref.shape[0]
    rows = [m_ref[i] for i in range(n)]
    for j in range(n):
        root = jnp.sqrt(rows[j][:, j:j + 1])
        pivot = rows[j] / root
        rows[j] = pivot
        scaled = pivot / root
        for i in range(j + 1, n):
            rows[i] = rows[i] - rows[i][:, j:j + 1] * scaled
    for i in range(n):
        o_ref[i] = rows[i][:, n:]


def block_inverses(gram):
    n = gram.shape[0] // BLOCK
    diag = jnp.stack([gram[b * BLOCK:(b + 1) * BLOCK, b * BLOCK:(b + 1) * BLOCK] for b in range(n)])
    eye = jnp.broadcast_to(jnp.eye(BLOCK, dtype=jnp.float32), diag.shape)
    aug = jnp.transpose(jnp.concatenate([diag, eye], axis=-1), (1, 0, 2))
    inv_lower = pl.pallas_call(
        _elim_kernel,
        out_shape=jax.ShapeDtypeStruct((BLOCK, n, BLOCK), jnp.float32),
    )(aug)
    return jnp.einsum("kbi,kbj->bji", inv_lower, inv_lower, precision=lax.Precision.HIGHEST)


def _partners(size, shift, m):
    return [(i, i ^ (m << shift)) for i in range(size)]


def radix4_scatter(x, axis, shifts):
    size = lax.axis_size(axis)
    idx = lax.axis_index(axis)
    cur = x
    for s in shifts:
        q = cur.shape[0] // 4
        digit = (idx >> s) & 3
        acc = lax.dynamic_slice_in_dim(cur, digit * q, q)
        for m in (1, 2, 3):
            send = lax.dynamic_slice_in_dim(cur, (digit ^ m) * q, q)
            acc = acc + lax.ppermute(send, axis, _partners(size, s, m))
        cur = acc
    return cur


def radix4_gather(x, axis, shifts):
    size = lax.axis_size(axis)
    idx = lax.axis_index(axis)
    cur = x
    for s in reversed(shifts):
        digit = (idx >> s) & 3
        got = [cur] + [lax.ppermute(cur, axis, _partners(size, s, m)) for m in (1, 2, 3)]
        pieces = []
        for p in range(4):
            rel = digit ^ p
            pieces.append(jnp.where(rel == 0, got[0], jnp.where(rel == 1, got[1], jnp.where(rel == 2, got[2], got[3]))))
        cur = jnp.concatenate(pieces)
    return cur


def _swap_grid(x):
    cols = x.shape[1]
    return x.reshape(4, 4, -1, cols).transpose(1, 0, 2, 3).reshape(-1, cols)


def balanced_scatter(x, axis, shifts):
    half = x.shape[1] // 2
    first = radix4_scatter(x[:, :half], axis, shifts)
    second = radix4_scatter(_swap_grid(x[:, half:]), axis, shifts[::-1])
    return jnp.concatenate([first, second], axis=1)


def balanced_gather(x, axis, shifts):
    half = x.shape[1] // 2
    first = radix4_gather(x[:, :half], axis, shifts)
    second = _swap_grid(radix4_gather(x[:, half:], axis, shifts[::-1]))
    return jnp.concatenate([first, second], axis=1)


def _sweep_kernel(ft_ref, ct_ref, g_ref, it_ref, o_ref):
    n = g_ref.shape[0] // BLOCK
    o_ref[...] = ft_ref[...]
    for b in range(n):
        lo, hi = b * BLOCK, (b + 1) * BLOCK
        prod = jnp.dot(g_ref[lo:hi, :], o_ref[...], precision=lax.Precision.HIGHEST, preferred_element_type=jnp.float32)
        resid = ct_ref[lo:hi, :] - prod
        step = jnp.dot(it_ref[b], resid, precision=lax.Precision.HIGHEST, preferred_element_type=jnp.float32)
        o_ref[lo:hi, :] = jnp.maximum(o_ref[lo:hi, :] + step, 0.0)


def block_sweep(factor, cross, gram, inverses_t):
    out_t = pl.pallas_call(
        _sweep_kernel,
        out_shape=jax.ShapeDtypeStruct((factor.shape[1], factor.shape[0]), jnp.float32),
    )(factor.T, cross.T, gram, inverses_t)
    return out_t.T


def shards(tfidf, occupancy, doc_factor, topic_factor):
    masked = mask_tiles(tfidf, occupancy)
    rows_group = lax.all_gather(doc_factor, "term", axis=0, tiled=True)
    gram_w = radix4_gather(
        radix4_scatter(
            lax.dot_general(rows_group, rows_group, (((0,), (0,)), ((), ())), preferred_element_type=jnp.float32),
            "doc",
            (0, 2),
        ),
        "doc",
        (0, 2),
    )
    inv_w = block_inverses(gram_w)
    cross_h = lax.psum_scatter(
        lax.dot_general(
            masked, rows_group, (((0,), (0,)), ((), ())), preferred_element_type=jnp.float32
        ),
        "doc",
        scatter_dimension=0,
        tiled=True,
    )
    new_topics = block_sweep(topic_factor.astype(jnp.float32), cross_h, gram_w, inv_w).astype(jnp.bfloat16)
    topic_group = lax.all_gather(new_topics, "doc", axis=0, tiled=True)
    cross_part = jnp.dot(masked, topic_group, preferred_element_type=jnp.float32)
    gram_part = lax.dot_general(topic_group, topic_group, (((0,), (0,)), ((), ())), preferred_element_type=jnp.float32)
    n_term = lax.axis_size("term")
    packed = jnp.stack(
        [cross_part.reshape(n_term, -1, cross_part.shape[1]), gram_part.reshape(n_term, -1, gram_part.shape[1])], axis=1
    ).reshape(-1, gram_part.shape[1])
    chunk = balanced_scatter(packed, "term", (2, 0))
    cross_w = chunk[: chunk.shape[0] // 2]
    gram_h = balanced_gather(chunk[chunk.shape[0] // 2:], "term", (2, 0))
    inv_h = block_inverses(gram_h)
    new_docs = block_sweep(doc_factor.astype(jnp.float32), cross_w, gram_h, inv_h).astype(jnp.bfloat16)
    return (new_docs, new_topics)


def solution(mesh):
    placed = (
        P("doc", "term"),
        P("doc", "term"),
        P(("doc", "term"), None),
        P(("term", "doc"), None),
    )
    return jax.shard_map(
        shards,
        mesh=mesh,
        in_specs=placed,
        out_specs=(P(("doc", "term"), None), P(("term", "doc"), None)),
        check_vma=False,
    )
```

```python
import jax
import jax.numpy as jnp
from jax import lax
from jax.experimental import pallas as pl
from jax.sharding import PartitionSpec as P

BLOCK = 64
TILE = 128


def mask_tiles(block, occ):
    rows, cols = block.shape
    tiles = block.reshape(rows // TILE, TILE, cols // TILE, TILE)
    tiles = tiles * occ.astype(jnp.bfloat16)[:, None, :, None]
    return tiles.reshape(rows, cols)


def _elim_kernel(m_ref, o_ref):
    n = m_ref.shape[0]
    rows = [m_ref[i] for i in range(n)]
    for j in range(n):
        root = jnp.sqrt(rows[j][:, j:j + 1])
        pivot = rows[j] / root
        rows[j] = pivot
        scaled = pivot / root
        for i in range(j + 1, n):
            rows[i] = rows[i] - rows[i][:, j:j + 1] * scaled
    for i in range(n):
        o_ref[i] = rows[i][:, n:]


def block_inverses(gram):
    n = gram.shape[0] // BLOCK
    diag = jnp.stack([gram[b * BLOCK:(b + 1) * BLOCK, b * BLOCK:(b + 1) * BLOCK] for b in range(n)])
    eye = jnp.broadcast_to(jnp.eye(BLOCK, dtype=jnp.float32), diag.shape)
    aug = jnp.transpose(jnp.concatenate([diag, eye], axis=-1), (1, 0, 2))
    inv_lower = pl.pallas_call(
        _elim_kernel,
        out_shape=jax.ShapeDtypeStruct((BLOCK, n, BLOCK), jnp.float32),
    )(aug)
    return jnp.einsum("kbi,kbj->bji", inv_lower, inv_lower, precision=lax.Precision.HIGHEST)


def _partners(size, shift, m):
    return [(i, i ^ (m << shift)) for i in range(size)]


def radix4_scatter(x, axis, shifts):
    size = lax.axis_size(axis)
    idx = lax.axis_index(axis)
    cur = x
    for s in shifts:
        q = cur.shape[0] // 4
        digit = (idx >> s) & 3
        acc = lax.dynamic_slice_in_dim(cur, digit * q, q)
        for m in (1, 2, 3):
            send = lax.dynamic_slice_in_dim(cur, (digit ^ m) * q, q)
            acc = acc + lax.ppermute(send, axis, _partners(size, s, m))
        cur = acc
    return cur


def radix4_gather(x, axis, shifts):
    size = lax.axis_size(axis)
    idx = lax.axis_index(axis)
    cur = x
    for s in reversed(shifts):
        digit = (idx >> s) & 3
        got = [cur] + [lax.ppermute(cur, axis, _partners(size, s, m)) for m in (1, 2, 3)]
        pieces = []
        for p in range(4):
            rel = digit ^ p
            pieces.append(jnp.where(rel == 0, got[0], jnp.where(rel == 1, got[1], jnp.where(rel == 2, got[2], got[3]))))
        cur = jnp.concatenate(pieces)
    return cur


def butterfly_psum(x, axis, order):
    size = lax.axis_size(axis)
    idx = lax.axis_index(axis)
    cur = x
    for k in order:
        half = cur.shape[0] // 2
        upper = ((idx >> k) & 1) == 1
        lo, hi = cur[:half], cur[half:]
        send = jnp.where(upper, lo, hi)
        keep = jnp.where(upper, hi, lo)
        got = lax.ppermute(send, axis, [(i, i ^ (1 << k)) for i in range(size)])
        cur = keep + got
    for k in reversed(order):
        upper = ((idx >> k) & 1) == 1
        got = lax.ppermute(cur, axis, [(i, i ^ (1 << k)) for i in range(size)])
        cur = jnp.where(upper, jnp.concatenate([got, cur]), jnp.concatenate([cur, got]))
    return cur


def _swap_grid(x):
    cols = x.shape[1]
    return x.reshape(4, 4, -1, cols).transpose(1, 0, 2, 3).reshape(-1, cols)


def balanced_scatter(x, axis, shifts):
    half = x.shape[1] // 2
    first = radix4_scatter(x[:, :half], axis, shifts)
    second = radix4_scatter(_swap_grid(x[:, half:]), axis, shifts[::-1])
    return jnp.concatenate([first, second], axis=1)


def balanced_gather(x, axis, shifts):
    half = x.shape[1] // 2
    first = radix4_gather(x[:, :half], axis, shifts)
    second = _swap_grid(radix4_gather(x[:, half:], axis, shifts[::-1]))
    return jnp.concatenate([first, second], axis=1)


def _sweep_kernel(ft_ref, ct_ref, g_ref, it_ref, o_ref):
    n = g_ref.shape[0] // BLOCK
    o_ref[...] = ft_ref[...]
    for b in range(n):
        lo, hi = b * BLOCK, (b + 1) * BLOCK
        prod = jnp.dot(g_ref[lo:hi, :], o_ref[...], precision=lax.Precision.HIGHEST, preferred_element_type=jnp.float32)
        resid = ct_ref[lo:hi, :] - prod
        step = jnp.dot(it_ref[b], resid, precision=lax.Precision.HIGHEST, preferred_element_type=jnp.float32)
        o_ref[lo:hi, :] = jnp.maximum(o_ref[lo:hi, :] + step, 0.0)


def block_sweep(factor, cross, gram, inverses_t):
    out_t = pl.pallas_call(
        _sweep_kernel,
        out_shape=jax.ShapeDtypeStruct((factor.shape[1], factor.shape[0]), jnp.float32),
    )(factor.T, cross.T, gram, inverses_t)
    return out_t.T


def shards(tfidf, occupancy, doc_factor, topic_factor):
    masked = mask_tiles(tfidf, occupancy)
    rows_group = lax.all_gather(doc_factor, "term", axis=0, tiled=True)
    gram_w = butterfly_psum(
        lax.dot_general(rows_group, rows_group, (((0,), (0,)), ((), ())), preferred_element_type=jnp.float32),
        "doc",
        (0, 1, 2, 3),
    )
    inv_w = block_inverses(gram_w)
    cross_h = lax.psum_scatter(
        lax.dot_general(
            masked, rows_group, (((0,), (0,)), ((), ())), preferred_element_type=jnp.float32
        ),
        "doc",
        scatter_dimension=0,
        tiled=True,
    )
    new_topics = block_sweep(topic_factor.astype(jnp.float32), cross_h, gram_w, inv_w).astype(jnp.bfloat16)
    topic_group = lax.all_gather(new_topics, "doc", axis=0, tiled=True)
    cross_part = jnp.dot(masked, topic_group, preferred_element_type=jnp.float32)
    gram_part = lax.dot_general(topic_group, topic_group, (((0,), (0,)), ((), ())), preferred_element_type=jnp.float32)
    n_term = lax.axis_size("term")
    packed = jnp.stack(
        [cross_part.reshape(n_term, -1, cross_part.shape[1]), gram_part.reshape(n_term, -1, gram_part.shape[1])], axis=1
    ).reshape(-1, gram_part.shape[1])
    chunk = balanced_scatter(packed, "term", (2, 0))
    cross_w = chunk[: chunk.shape[0] // 2]
    gram_h = balanced_gather(chunk[chunk.shape[0] // 2:], "term", (2, 0))
    inv_h = block_inverses(gram_h)
    new_docs = block_sweep(doc_factor.astype(jnp.float32), cross_w, gram_h, inv_h).astype(jnp.bfloat16)
    return (new_docs, new_topics)


def solution(mesh):
    placed = (
        P("doc", "term"),
        P("doc", "term"),
        P(("doc", "term"), None),
        P(("term", "doc"), None),
    )
    return jax.shard_map(
        shards,
        mesh=mesh,
        in_specs=placed,
        out_specs=(P(("doc", "term"), None), P(("term", "doc"), None)),
        check_vma=False,
    )
```

```python
import jax
import jax.numpy as jnp
from jax import lax
from jax.experimental import pallas as pl
from jax.sharding import PartitionSpec as P

BLOCK = 64
TILE = 128


def mask_tiles(block, occ):
    rows, cols = block.shape
    tiles = block.reshape(rows // TILE, TILE, cols // TILE, TILE)
    tiles = tiles * occ.astype(jnp.bfloat16)[:, None, :, None]
    return tiles.reshape(rows, cols)


def _elim_kernel(m_ref, o_ref):
    n = m_ref.shape[0]
    rows = [m_ref[i] for i in range(n)]
    for j in range(n):
        root = jnp.sqrt(rows[j][:, j:j + 1])
        pivot = rows[j] / root
        rows[j] = pivot
        scaled = pivot / root
        for i in range(j + 1, n):
            rows[i] = rows[i] - rows[i][:, j:j + 1] * scaled
    for i in range(n):
        o_ref[i] = rows[i][:, n:]


def block_inverses(gram):
    n = gram.shape[0] // BLOCK
    diag = jnp.stack([gram[b * BLOCK:(b + 1) * BLOCK, b * BLOCK:(b + 1) * BLOCK] for b in range(n)])
    eye = jnp.broadcast_to(jnp.eye(BLOCK, dtype=jnp.float32), diag.shape)
    aug = jnp.transpose(jnp.concatenate([diag, eye], axis=-1), (1, 0, 2))
    inv_lower = pl.pallas_call(
        _elim_kernel,
        out_shape=jax.ShapeDtypeStruct((BLOCK, n, BLOCK), jnp.float32),
    )(aug)
    return jnp.einsum("kbi,kbj->bji", inv_lower, inv_lower, precision=lax.Precision.HIGHEST)


def _partners(size, shift, m):
    return [(i, i ^ (m << shift)) for i in range(size)]


def radix4_scatter(x, axis, shifts):
    size = lax.axis_size(axis)
    idx = lax.axis_index(axis)
    cur = x
    for s in shifts:
        q = cur.shape[0] // 4
        digit = (idx >> s) & 3
        acc = lax.dynamic_slice_in_dim(cur, digit * q, q)
        for m in (1, 2, 3):
            send = lax.dynamic_slice_in_dim(cur, (digit ^ m) * q, q)
            acc = acc + lax.ppermute(send, axis, _partners(size, s, m))
        cur = acc
    return cur


def radix4_gather(x, axis, shifts):
    size = lax.axis_size(axis)
    idx = lax.axis_index(axis)
    cur = x
    for s in reversed(shifts):
        digit = (idx >> s) & 3
        got = [cur] + [lax.ppermute(cur, axis, _partners(size, s, m)) for m in (1, 2, 3)]
        pieces = []
        for p in range(4):
            rel = digit ^ p
            pieces.append(jnp.where(rel == 0, got[0], jnp.where(rel == 1, got[1], jnp.where(rel == 2, got[2], got[3]))))
        cur = jnp.concatenate(pieces)
    return cur


def butterfly_psum(x, axis, order):
    size = lax.axis_size(axis)
    idx = lax.axis_index(axis)
    cur = x
    for k in order:
        half = cur.shape[0] // 2
        upper = ((idx >> k) & 1) == 1
        lo, hi = cur[:half], cur[half:]
        send = jnp.where(upper, lo, hi)
        keep = jnp.where(upper, hi, lo)
        got = lax.ppermute(send, axis, [(i, i ^ (1 << k)) for i in range(size)])
        cur = keep + got
    for k in reversed(order):
        upper = ((idx >> k) & 1) == 1
        got = lax.ppermute(cur, axis, [(i, i ^ (1 << k)) for i in range(size)])
        cur = jnp.where(upper, jnp.concatenate([got, cur]), jnp.concatenate([cur, got]))
    return cur


def butterfly_scatter(x, axis, order):
    size = lax.axis_size(axis)
    idx = lax.axis_index(axis)
    place = [sum(((k >> b) & 1) << (len(order) - 1 - t) for t, b in enumerate(order)) for k in range(size)]
    owner = [place.index(p) for p in range(size)]
    chunks = x.reshape(size, -1, x.shape[1])
    cur = jnp.concatenate([chunks[k] for k in owner])
    for k in order:
        half = cur.shape[0] // 2
        upper = ((idx >> k) & 1) == 1
        lo, hi = cur[:half], cur[half:]
        send = jnp.where(upper, lo, hi)
        keep = jnp.where(upper, hi, lo)
        cur = keep + lax.ppermute(send, axis, [(i, i ^ (1 << k)) for i in range(size)])
    return cur


def _swap_grid(x):
    cols = x.shape[1]
    return x.reshape(4, 4, -1, cols).transpose(1, 0, 2, 3).reshape(-1, cols)


def balanced_scatter(x, axis, shifts):
    half = x.shape[1] // 2
    first = radix4_scatter(x[:, :half], axis, shifts)
    second = radix4_scatter(_swap_grid(x[:, half:]), axis, shifts[::-1])
    return jnp.concatenate([first, second], axis=1)


def balanced_gather(x, axis, shifts):
    half = x.shape[1] // 2
    first = radix4_gather(x[:, :half], axis, shifts)
    second = _swap_grid(radix4_gather(x[:, half:], axis, shifts[::-1]))
    return jnp.concatenate([first, second], axis=1)


def _sweep_kernel(ft_ref, ct_ref, g_ref, it_ref, o_ref):
    n = g_ref.shape[0] // BLOCK
    o_ref[...] = ft_ref[...]
    for b in range(n):
        lo, hi = b * BLOCK, (b + 1) * BLOCK
        prod = jnp.dot(g_ref[lo:hi, :], o_ref[...], precision=lax.Precision.HIGHEST, preferred_element_type=jnp.float32)
        resid = ct_ref[lo:hi, :] - prod
        step = jnp.dot(it_ref[b], resid, precision=lax.Precision.HIGHEST, preferred_element_type=jnp.float32)
        o_ref[lo:hi, :] = jnp.maximum(o_ref[lo:hi, :] + step, 0.0)


def block_sweep(factor, cross, gram, inverses_t):
    out_t = pl.pallas_call(
        _sweep_kernel,
        out_shape=jax.ShapeDtypeStruct((factor.shape[1], factor.shape[0]), jnp.float32),
    )(factor.T, cross.T, gram, inverses_t)
    return out_t.T


def shards(tfidf, occupancy, doc_factor, topic_factor):
    masked = mask_tiles(tfidf, occupancy)
    rows_group = lax.all_gather(doc_factor, "term", axis=0, tiled=True)
    gram_w = butterfly_psum(
        lax.dot_general(rows_group, rows_group, (((0,), (0,)), ((), ())), preferred_element_type=jnp.float32),
        "doc",
        (0, 1, 2, 3),
    )
    inv_w = block_inverses(gram_w)
    cross_full = lax.dot_general(masked, rows_group, (((0,), (0,)), ((), ())), preferred_element_type=jnp.float32)
    half = cross_full.shape[1] // 2
    cross_h = jnp.concatenate(
        [
            lax.psum_scatter(cross_full[:, :half], "doc", scatter_dimension=0, tiled=True),
            butterfly_scatter(cross_full[:, half:], "doc", (0, 1, 2, 3)),
        ],
        axis=1,
    )
    new_topics = block_sweep(topic_factor.astype(jnp.float32), cross_h, gram_w, inv_w).astype(jnp.bfloat16)
    topic_group = lax.all_gather(new_topics, "doc", axis=0, tiled=True)
    cross_part = jnp.dot(masked, topic_group, preferred_element_type=jnp.float32)
    gram_part = lax.dot_general(topic_group, topic_group, (((0,), (0,)), ((), ())), preferred_element_type=jnp.float32)
    n_term = lax.axis_size("term")
    packed = jnp.stack(
        [cross_part.reshape(n_term, -1, cross_part.shape[1]), gram_part.reshape(n_term, -1, gram_part.shape[1])], axis=1
    ).reshape(-1, gram_part.shape[1])
    chunk = balanced_scatter(packed, "term", (2, 0))
    cross_w = chunk[: chunk.shape[0] // 2]
    gram_h = balanced_gather(chunk[chunk.shape[0] // 2:], "term", (2, 0))
    inv_h = block_inverses(gram_h)
    new_docs = block_sweep(doc_factor.astype(jnp.float32), cross_w, gram_h, inv_h).astype(jnp.bfloat16)
    return (new_docs, new_topics)


def solution(mesh):
    placed = (
        P("doc", "term"),
        P("doc", "term"),
        P(("doc", "term"), None),
        P(("term", "doc"), None),
    )
    return jax.shard_map(
        shards,
        mesh=mesh,
        in_specs=placed,
        out_specs=(P(("doc", "term"), None), P(("term", "doc"), None)),
        check_vma=False,
    )
```

```python
import jax
import jax.numpy as jnp
from jax import lax
from jax.experimental import pallas as pl
from jax.sharding import PartitionSpec as P

BLOCK = 64
TILE = 128


def mask_tiles(block, occ):
    rows, cols = block.shape
    tiles = block.reshape(rows // TILE, TILE, cols // TILE, TILE)
    tiles = tiles * occ.astype(jnp.bfloat16)[:, None, :, None]
    return tiles.reshape(rows, cols)


def _elim_kernel(m_ref, o_ref):
    n = m_ref.shape[0]
    rows = [m_ref[i] for i in range(n)]
    for j in range(n):
        root = jnp.sqrt(rows[j][:, j:j + 1])
        pivot = rows[j] / root
        rows[j] = pivot
        scaled = pivot / root
        for i in range(j + 1, n):
            rows[i] = rows[i] - rows[i][:, j:j + 1] * scaled
    for i in range(n):
        o_ref[i] = rows[i][:, n:]


def block_inverses(gram):
    n = gram.shape[0] // BLOCK
    diag = jnp.stack([gram[b * BLOCK:(b + 1) * BLOCK, b * BLOCK:(b + 1) * BLOCK] for b in range(n)])
    eye = jnp.broadcast_to(jnp.eye(BLOCK, dtype=jnp.float32), diag.shape)
    aug = jnp.transpose(jnp.concatenate([diag, eye], axis=-1), (1, 0, 2))
    inv_lower = pl.pallas_call(
        _elim_kernel,
        out_shape=jax.ShapeDtypeStruct((BLOCK, n, BLOCK), jnp.float32),
    )(aug)
    return jnp.einsum("kbi,kbj->bji", inv_lower, inv_lower, precision=lax.Precision.HIGHEST)


def _partners(size, shift, m):
    return [(i, i ^ (m << shift)) for i in range(size)]


def radix4_scatter(x, axis, shifts):
    size = lax.axis_size(axis)
    idx = lax.axis_index(axis)
    cur = x
    for s in shifts:
        q = cur.shape[0] // 4
        digit = (idx >> s) & 3
        acc = lax.dynamic_slice_in_dim(cur, digit * q, q)
        for m in (1, 2, 3):
            send = lax.dynamic_slice_in_dim(cur, (digit ^ m) * q, q)
            acc = acc + lax.ppermute(send, axis, _partners(size, s, m))
        cur = acc
    return cur


def radix4_gather(x, axis, shifts):
    size = lax.axis_size(axis)
    idx = lax.axis_index(axis)
    cur = x
    for s in reversed(shifts):
        digit = (idx >> s) & 3
        got = [cur] + [lax.ppermute(cur, axis, _partners(size, s, m)) for m in (1, 2, 3)]
        pieces = []
        for p in range(4):
            rel = digit ^ p
            pieces.append(jnp.where(rel == 0, got[0], jnp.where(rel == 1, got[1], jnp.where(rel == 2, got[2], got[3]))))
        cur = jnp.concatenate(pieces)
    return cur


def butterfly_psum(x, axis, order):
    size = lax.axis_size(axis)
    idx = lax.axis_index(axis)
    cur = x
    for k in order:
        half = cur.shape[0] // 2
        upper = ((idx >> k) & 1) == 1
        lo, hi = cur[:half], cur[half:]
        send = jnp.where(upper, lo, hi)
        keep = jnp.where(upper, hi, lo)
        got = lax.ppermute(send, axis, [(i, i ^ (1 << k)) for i in range(size)])
        cur = keep + got
    for k in reversed(order):
        upper = ((idx >> k) & 1) == 1
        got = lax.ppermute(cur, axis, [(i, i ^ (1 << k)) for i in range(size)])
        cur = jnp.where(upper, jnp.concatenate([got, cur]), jnp.concatenate([cur, got]))
    return cur


def doubling_gather(x, axis, order):
    size = lax.axis_size(axis)
    idx = lax.axis_index(axis)
    cur = x
    for k in order:
        upper = ((idx >> k) & 1) == 1
        got = lax.ppermute(cur, axis, [(i, i ^ (1 << k)) for i in range(size)])
        cur = jnp.where(upper, jnp.concatenate([got, cur]), jnp.concatenate([cur, got]))
    place = [sum(((k >> b) & 1) << t for t, b in enumerate(order)) for k in range(size)]
    chunks = cur.reshape(size, -1, cur.shape[1])
    return jnp.concatenate([chunks[place[k]] for k in range(size)])


def _swap_grid(x):
    cols = x.shape[1]
    return x.reshape(4, 4, -1, cols).transpose(1, 0, 2, 3).reshape(-1, cols)


def balanced_scatter(x, axis, shifts):
    half = x.shape[1] // 2
    first = radix4_scatter(x[:, :half], axis, shifts)
    second = radix4_scatter(_swap_grid(x[:, half:]), axis, shifts[::-1])
    return jnp.concatenate([first, second], axis=1)


def balanced_gather(x, axis, shifts):
    half = x.shape[1] // 2
    first = radix4_gather(x[:, :half], axis, shifts)
    second = _swap_grid(radix4_gather(x[:, half:], axis, shifts[::-1]))
    return jnp.concatenate([first, second], axis=1)


def _sweep_kernel(ft_ref, ct_ref, g_ref, it_ref, o_ref):
    n = g_ref.shape[0] // BLOCK
    o_ref[...] = ft_ref[...]
    for b in range(n):
        lo, hi = b * BLOCK, (b + 1) * BLOCK
        prod = jnp.dot(g_ref[lo:hi, :], o_ref[...], precision=lax.Precision.HIGHEST, preferred_element_type=jnp.float32)
        resid = ct_ref[lo:hi, :] - prod
        step = jnp.dot(it_ref[b], resid, precision=lax.Precision.HIGHEST, preferred_element_type=jnp.float32)
        o_ref[lo:hi, :] = jnp.maximum(o_ref[lo:hi, :] + step, 0.0)


def block_sweep(factor, cross, gram, inverses_t):
    out_t = pl.pallas_call(
        _sweep_kernel,
        out_shape=jax.ShapeDtypeStruct((factor.shape[1], factor.shape[0]), jnp.float32),
    )(factor.T, cross.T, gram, inverses_t)
    return out_t.T


def shards(tfidf, occupancy, doc_factor, topic_factor):
    masked = mask_tiles(tfidf, occupancy)
    rows_group = lax.all_gather(doc_factor, "term", axis=0, tiled=True)
    gram_w = butterfly_psum(
        lax.dot_general(rows_group, rows_group, (((0,), (0,)), ((), ())), preferred_element_type=jnp.float32),
        "doc",
        (0, 1, 2, 3),
    )
    inv_w = block_inverses(gram_w)
    cross_h = lax.psum_scatter(
        lax.dot_general(
            masked, rows_group, (((0,), (0,)), ((), ())), preferred_element_type=jnp.float32
        ),
        "doc",
        scatter_dimension=0,
        tiled=True,
    )
    new_topics = block_sweep(topic_factor.astype(jnp.float32), cross_h, gram_w, inv_w).astype(jnp.bfloat16)
    topic_group = doubling_gather(new_topics, "doc", (3, 2, 1, 0))
    cross_part = jnp.dot(masked, topic_group, preferred_element_type=jnp.float32)
    gram_part = lax.dot_general(topic_group, topic_group, (((0,), (0,)), ((), ())), preferred_element_type=jnp.float32)
    n_term = lax.axis_size("term")
    packed = jnp.stack(
        [cross_part.reshape(n_term, -1, cross_part.shape[1]), gram_part.reshape(n_term, -1, gram_part.shape[1])], axis=1
    ).reshape(-1, gram_part.shape[1])
    chunk = balanced_scatter(packed, "term", (2, 0))
    cross_w = chunk[: chunk.shape[0] // 2]
    gram_h = balanced_gather(chunk[chunk.shape[0] // 2:], "term", (2, 0))
    inv_h = block_inverses(gram_h)
    new_docs = block_sweep(doc_factor.astype(jnp.float32), cross_w, gram_h, inv_h).astype(jnp.bfloat16)
    return (new_docs, new_topics)


def solution(mesh):
    placed = (
        P("doc", "term"),
        P("doc", "term"),
        P(("doc", "term"), None),
        P(("term", "doc"), None),
    )
    return jax.shard_map(
        shards,
        mesh=mesh,
        in_specs=placed,
        out_specs=(P(("doc", "term"), None), P(("term", "doc"), None)),
        check_vma=False,
    )
```

```python
import jax
import jax.numpy as jnp
from jax import lax
from jax.experimental import pallas as pl
from jax.sharding import PartitionSpec as P

BLOCK = 64
TILE = 128


def mask_tiles(block, occ):
    rows, cols = block.shape
    tiles = block.reshape(rows // TILE, TILE, cols // TILE, TILE)
    tiles = tiles * occ.astype(jnp.bfloat16)[:, None, :, None]
    return tiles.reshape(rows, cols)


def _elim_kernel(m_ref, o_ref):
    n = m_ref.shape[0]
    rows = [m_ref[i] for i in range(n)]
    for j in range(n):
        root = jnp.sqrt(rows[j][:, j:j + 1])
        pivot = rows[j] / root
        rows[j] = pivot
        scaled = pivot / root
        for i in range(j + 1, n):
            rows[i] = rows[i] - rows[i][:, j:j + 1] * scaled
    for i in range(n):
        o_ref[i] = rows[i][:, n:]


def diagonal_blocks(gram):
    n = gram.shape[0] // BLOCK
    return jnp.stack([gram[b * BLOCK:(b + 1) * BLOCK, b * BLOCK:(b + 1) * BLOCK] for b in range(n)])


def block_inverses(gram):
    return diag_inverses(diagonal_blocks(gram))


def diag_inverses(diag):
    n = diag.shape[0]
    eye = jnp.broadcast_to(jnp.eye(BLOCK, dtype=jnp.float32), diag.shape)
    aug = jnp.transpose(jnp.concatenate([diag, eye], axis=-1), (1, 0, 2))
    inv_lower = pl.pallas_call(
        _elim_kernel,
        out_shape=jax.ShapeDtypeStruct((BLOCK, n, BLOCK), jnp.float32),
    )(aug)
    return jnp.einsum("kbi,kbj->bji", inv_lower, inv_lower, precision=lax.Precision.HIGHEST)


def _partners(size, shift, m):
    return [(i, i ^ (m << shift)) for i in range(size)]


def radix4_scatter(x, axis, shifts):
    size = lax.axis_size(axis)
    idx = lax.axis_index(axis)
    cur = x
    for s in shifts:
        q = cur.shape[0] // 4
        digit = (idx >> s) & 3
        acc = lax.dynamic_slice_in_dim(cur, digit * q, q)
        for m in (1, 2, 3):
            send = lax.dynamic_slice_in_dim(cur, (digit ^ m) * q, q)
            acc = acc + lax.ppermute(send, axis, _partners(size, s, m))
        cur = acc
    return cur


def radix4_gather(x, axis, shifts):
    size = lax.axis_size(axis)
    idx = lax.axis_index(axis)
    cur = x
    for s in reversed(shifts):
        digit = (idx >> s) & 3
        got = [cur] + [lax.ppermute(cur, axis, _partners(size, s, m)) for m in (1, 2, 3)]
        pieces = []
        for p in range(4):
            rel = digit ^ p
            pieces.append(jnp.where(rel == 0, got[0], jnp.where(rel == 1, got[1], jnp.where(rel == 2, got[2], got[3]))))
        cur = jnp.concatenate(pieces)
    return cur


def butterfly_psum(x, axis, order):
    size = lax.axis_size(axis)
    idx = lax.axis_index(axis)
    cur = x
    for k in order:
        half = cur.shape[0] // 2
        upper = ((idx >> k) & 1) == 1
        lo, hi = cur[:half], cur[half:]
        send = jnp.where(upper, lo, hi)
        keep = jnp.where(upper, hi, lo)
        got = lax.ppermute(send, axis, [(i, i ^ (1 << k)) for i in range(size)])
        cur = keep + got
    for k in reversed(order):
        upper = ((idx >> k) & 1) == 1
        got = lax.ppermute(cur, axis, [(i, i ^ (1 << k)) for i in range(size)])
        cur = jnp.where(upper, jnp.concatenate([got, cur]), jnp.concatenate([cur, got]))
    return cur


def _swap_grid(x):
    cols = x.shape[1]
    return x.reshape(4, 4, -1, cols).transpose(1, 0, 2, 3).reshape(-1, cols)


def balanced_scatter(x, axis, shifts):
    half = x.shape[1] // 2
    first = radix4_scatter(x[:, :half], axis, shifts)
    second = radix4_scatter(_swap_grid(x[:, half:]), axis, shifts[::-1])
    return jnp.concatenate([first, second], axis=1)


def balanced_gather(x, axis, shifts):
    half = x.shape[1] // 2
    first = radix4_gather(x[:, :half], axis, shifts)
    second = _swap_grid(radix4_gather(x[:, half:], axis, shifts[::-1]))
    return jnp.concatenate([first, second], axis=1)


def _sweep_kernel(ft_ref, ct_ref, g_ref, it_ref, o_ref):
    n = g_ref.shape[0] // BLOCK
    o_ref[...] = ft_ref[...]
    for b in range(n):
        lo, hi = b * BLOCK, (b + 1) * BLOCK
        prod = jnp.dot(g_ref[lo:hi, :], o_ref[...], precision=lax.Precision.HIGHEST, preferred_element_type=jnp.float32)
        resid = ct_ref[lo:hi, :] - prod
        step = jnp.dot(it_ref[b], resid, precision=lax.Precision.HIGHEST, preferred_element_type=jnp.float32)
        o_ref[lo:hi, :] = jnp.maximum(o_ref[lo:hi, :] + step, 0.0)


def block_sweep(factor, cross, gram, inverses_t):
    out_t = pl.pallas_call(
        _sweep_kernel,
        out_shape=jax.ShapeDtypeStruct((factor.shape[1], factor.shape[0]), jnp.float32),
    )(factor.T, cross.T, gram, inverses_t)
    return out_t.T


def shards(tfidf, occupancy, doc_factor, topic_factor):
    masked = mask_tiles(tfidf, occupancy)
    rows_group = lax.all_gather(doc_factor, "term", axis=0, tiled=True)
    gram_part = lax.dot_general(rows_group, rows_group, (((0,), (0,)), ((), ())), preferred_element_type=jnp.float32)
    diag_part = diagonal_blocks(gram_part)
    diag_w = butterfly_psum(diag_part.reshape(-1, BLOCK), "doc", (0, 1, 2, 3)).reshape(diag_part.shape)
    gram_w = butterfly_psum(gram_part, "doc", (0, 1, 2, 3))
    inv_w = diag_inverses(diag_w)
    cross_h = lax.psum_scatter(
        lax.dot_general(
            masked, rows_group, (((0,), (0,)), ((), ())), preferred_element_type=jnp.float32
        ),
        "doc",
        scatter_dimension=0,
        tiled=True,
    )
    new_topics = block_sweep(topic_factor.astype(jnp.float32), cross_h, gram_w, inv_w).astype(jnp.bfloat16)
    topic_group = lax.all_gather(new_topics, "doc", axis=0, tiled=True)
    cross_part = jnp.dot(masked, topic_group, preferred_element_type=jnp.float32)
    gram_part = lax.dot_general(topic_group, topic_group, (((0,), (0,)), ((), ())), preferred_element_type=jnp.float32)
    n_term = lax.axis_size("term")
    packed = jnp.stack(
        [cross_part.reshape(n_term, -1, cross_part.shape[1]), gram_part.reshape(n_term, -1, gram_part.shape[1])], axis=1
    ).reshape(-1, gram_part.shape[1])
    chunk = balanced_scatter(packed, "term", (2, 0))
    cross_w = chunk[: chunk.shape[0] // 2]
    gram_h = balanced_gather(chunk[chunk.shape[0] // 2:], "term", (2, 0))
    inv_h = block_inverses(gram_h)
    new_docs = block_sweep(doc_factor.astype(jnp.float32), cross_w, gram_h, inv_h).astype(jnp.bfloat16)
    return (new_docs, new_topics)


def solution(mesh):
    placed = (
        P("doc", "term"),
        P("doc", "term"),
        P(("doc", "term"), None),
        P(("term", "doc"), None),
    )
    return jax.shard_map(
        shards,
        mesh=mesh,
        in_specs=placed,
        out_specs=(P(("doc", "term"), None), P(("term", "doc"), None)),
        check_vma=False,
    )
```

```python
import jax
import jax.numpy as jnp
from jax import lax
from jax.experimental import pallas as pl
from jax.experimental.pallas import tpu as pltpu
from jax.sharding import PartitionSpec as P

BLOCK = 64
TILE = 128


def mask_tiles(block, occ):
    rows, cols = block.shape
    tiles = block.reshape(rows // TILE, TILE, cols // TILE, TILE)
    tiles = tiles * occ.astype(jnp.bfloat16)[:, None, :, None]
    return tiles.reshape(rows, cols)


def _elim_kernel(m_ref, o_ref):
    n = m_ref.shape[0]
    rows = [m_ref[i] for i in range(n)]
    for j in range(n):
        root = jnp.sqrt(rows[j][:, j:j + 1])
        pivot = rows[j] / root
        rows[j] = pivot
        scaled = pivot / root
        for i in range(j + 1, n):
            rows[i] = rows[i] - rows[i][:, j:j + 1] * scaled
    for i in range(n):
        o_ref[i] = rows[i][:, n:]


def block_inverses(gram):
    n = gram.shape[0] // BLOCK
    diag = jnp.stack([gram[b * BLOCK:(b + 1) * BLOCK, b * BLOCK:(b + 1) * BLOCK] for b in range(n)])
    eye = jnp.broadcast_to(jnp.eye(BLOCK, dtype=jnp.float32), diag.shape)
    aug = jnp.transpose(jnp.concatenate([diag, eye], axis=-1), (1, 0, 2))
    inv_lower = pl.pallas_call(
        _elim_kernel,
        out_shape=jax.ShapeDtypeStruct((BLOCK, n, BLOCK), jnp.float32),
    )(aug)
    return jnp.einsum("kbi,kbj->bji", inv_lower, inv_lower, precision=lax.Precision.HIGHEST)


def _partners(size, shift, m):
    return [(i, i ^ (m << shift)) for i in range(size)]


def radix4_scatter(x, axis, shifts):
    size = lax.axis_size(axis)
    idx = lax.axis_index(axis)
    cur = x
    for s in shifts:
        q = cur.shape[0] // 4
        digit = (idx >> s) & 3
        acc = lax.dynamic_slice_in_dim(cur, digit * q, q)
        for m in (1, 2, 3):
            send = lax.dynamic_slice_in_dim(cur, (digit ^ m) * q, q)
            acc = acc + lax.ppermute(send, axis, _partners(size, s, m))
        cur = acc
    return cur


def radix4_gather(x, axis, shifts):
    size = lax.axis_size(axis)
    idx = lax.axis_index(axis)
    cur = x
    for s in reversed(shifts):
        digit = (idx >> s) & 3
        got = [cur] + [lax.ppermute(cur, axis, _partners(size, s, m)) for m in (1, 2, 3)]
        pieces = []
        for p in range(4):
            rel = digit ^ p
            pieces.append(jnp.where(rel == 0, got[0], jnp.where(rel == 1, got[1], jnp.where(rel == 2, got[2], got[3]))))
        cur = jnp.concatenate(pieces)
    return cur


def butterfly_psum(x, axis, order):
    size = lax.axis_size(axis)
    idx = lax.axis_index(axis)
    cur = x
    for k in order:
        half = cur.shape[0] // 2
        upper = ((idx >> k) & 1) == 1
        lo, hi = cur[:half], cur[half:]
        send = jnp.where(upper, lo, hi)
        keep = jnp.where(upper, hi, lo)
        got = lax.ppermute(send, axis, [(i, i ^ (1 << k)) for i in range(size)])
        cur = keep + got
    for k in reversed(order):
        upper = ((idx >> k) & 1) == 1
        got = lax.ppermute(cur, axis, [(i, i ^ (1 << k)) for i in range(size)])
        cur = jnp.where(upper, jnp.concatenate([got, cur]), jnp.concatenate([cur, got]))
    return cur


def _swap_grid(x):
    cols = x.shape[1]
    return x.reshape(4, 4, -1, cols).transpose(1, 0, 2, 3).reshape(-1, cols)


def balanced_scatter(x, axis, shifts):
    half = x.shape[1] // 2
    first = radix4_scatter(x[:, :half], axis, shifts)
    second = radix4_scatter(_swap_grid(x[:, half:]), axis, shifts[::-1])
    return jnp.concatenate([first, second], axis=1)


def balanced_gather(x, axis, shifts):
    half = x.shape[1] // 2
    first = radix4_gather(x[:, :half], axis, shifts)
    second = _swap_grid(radix4_gather(x[:, half:], axis, shifts[::-1]))
    return jnp.concatenate([first, second], axis=1)


def _sweep_kernel(ft_ref, ct_ref, g_ref, it_ref, o_ref, f_ref):
    n = g_ref.shape[0] // BLOCK
    f_ref[...] = ft_ref[...].astype(jnp.float32)
    for b in range(n):
        lo, hi = b * BLOCK, (b + 1) * BLOCK
        prod = jnp.dot(g_ref[lo:hi, :], f_ref[...], precision=lax.Precision.HIGHEST, preferred_element_type=jnp.float32)
        resid = ct_ref[lo:hi, :] - prod
        step = jnp.dot(it_ref[b], resid, precision=lax.Precision.HIGHEST, preferred_element_type=jnp.float32)
        f_ref[lo:hi, :] = jnp.maximum(f_ref[lo:hi, :] + step, 0.0)
    o_ref[...] = f_ref[...].astype(o_ref.dtype)


def block_sweep(factor, cross, gram, inverses_t):
    out_t = pl.pallas_call(
        _sweep_kernel,
        out_shape=jax.ShapeDtypeStruct((factor.shape[1], factor.shape[0]), jnp.bfloat16),
        scratch_shapes=[pltpu.VMEM((factor.shape[1], factor.shape[0]), jnp.float32)],
    )(factor.T, cross.T, gram, inverses_t)
    return out_t.T


def shards(tfidf, occupancy, doc_factor, topic_factor):
    masked = mask_tiles(tfidf, occupancy)
    rows_group = lax.all_gather(doc_factor, "term", axis=0, tiled=True)
    gram_w = butterfly_psum(
        lax.dot_general(rows_group, rows_group, (((0,), (0,)), ((), ())), preferred_element_type=jnp.float32),
        "doc",
        (0, 1, 2, 3),
    )
    inv_w = block_inverses(gram_w)
    cross_h = lax.psum_scatter(
        lax.dot_general(
            masked, rows_group, (((0,), (0,)), ((), ())), preferred_element_type=jnp.float32
        ),
        "doc",
        scatter_dimension=0,
        tiled=True,
    )
    new_topics = block_sweep(topic_factor, cross_h, gram_w, inv_w)
    topic_group = lax.all_gather(new_topics, "doc", axis=0, tiled=True)
    cross_part = jnp.dot(masked, topic_group, preferred_element_type=jnp.float32)
    gram_part = lax.dot_general(topic_group, topic_group, (((0,), (0,)), ((), ())), preferred_element_type=jnp.float32)
    n_term = lax.axis_size("term")
    packed = jnp.stack(
        [cross_part.reshape(n_term, -1, cross_part.shape[1]), gram_part.reshape(n_term, -1, gram_part.shape[1])], axis=1
    ).reshape(-1, gram_part.shape[1])
    chunk = balanced_scatter(packed, "term", (2, 0))
    cross_w = chunk[: chunk.shape[0] // 2]
    gram_h = balanced_gather(chunk[chunk.shape[0] // 2:], "term", (2, 0))
    inv_h = block_inverses(gram_h)
    new_docs = block_sweep(doc_factor, cross_w, gram_h, inv_h)
    return (new_docs, new_topics)


def solution(mesh):
    placed = (
        P("doc", "term"),
        P("doc", "term"),
        P(("doc", "term"), None),
        P(("term", "doc"), None),
    )
    return jax.shard_map(
        shards,
        mesh=mesh,
        in_specs=placed,
        out_specs=(P(("doc", "term"), None), P(("term", "doc"), None)),
        check_vma=False,
    )
```
